512 devices in a mesh: freq: 16 (over y, core), trace: 32 (over z, x).
Axes of the slice: x: 4, y: 8, z: 8, core: 2. Of those that a mesh axis runs over, the one named last changes fastest.
Arguments:
- traces: bfloat16 [64, 128, 2048], P('trace', 'freq'), may hold values from -20 to 20
- omega: float32 [2, 33, 64, 64], replicated, may hold values from -0.125 to 0.125
Outputs:
- denoised: float32 [64, 128, 2048], P('trace', 'freq')
The draws below stay inside these ranges and needn't reach their ends.
All inputs are finite; a program needn't handle non-finite values.
Results may differ from the reference program's by a relative error of at most 0.0003.
Values sent between devices are 32-bit elements; how exact they have to be, the bound alone decides.
No kernel may reach another device: no remote copies, remote signals or barrier semaphores. Data moves between devices by JAX's collectives and lax.ppermute only.
A program may use at most 64 MiB of HBM per device.

```python
import math
import jax
import jax.numpy as jnp
from jax import lax

SAMPLES = 2048
RANK = 64
PATCH_X = 64
PATCH_Y = 128
LAG_X = 33
WIN_X = 32
LAG_Y = 64
WIN_Y = 65
FREQS = 16


event_count = 80


def draw_traces(key, part):
    subkeys = jax.random.split(key, 6)
    onsets = jax.random.uniform(subkeys[0], (event_count,), jnp.float32, 0.25 * SAMPLES, 0.75 * SAMPLES)
    moveout = 0.1 * SAMPLES
    dips_x = jax.random.uniform(subkeys[1], (event_count,), jnp.float32, -1.0, 1.0) * (moveout / PATCH_X)
    dips_y = jax.random.uniform(subkeys[2], (event_count,), jnp.float32, -1.0, 1.0) * (moveout / PATCH_Y)
    levels = jnp.exp(jax.random.uniform(subkeys[3], (event_count,), jnp.float32, math.log(0.01), math.log(0.12)))
    polarity = jax.random.randint(subkeys[4], (event_count,), 0, 2).astype(jnp.float32) * 2.0 - 1.0
    heights = levels * polarity
    sharpness = math.pi * 0.5 * FREQS / SAMPLES
    across = (jnp.arange(PATCH_X, dtype=jnp.float32) - 0.5 * PATCH_X)[:, None, None]
    inline_pos = (jnp.arange(PATCH_Y, dtype=jnp.float32) - 0.5 * PATCH_Y)[None, :, None]
    moments = jnp.arange(SAMPLES, dtype=jnp.float32)[None, None, :]

    def add_event(event_index, signal):
        arrival = onsets[event_index] + dips_x[event_index] * across + dips_y[event_index] * inline_pos
        scaled = sharpness * (moments - arrival)
        squared = scaled * scaled
        return signal + heights[event_index] * (1.0 - 2.0 * squared) * jnp.exp(-squared)
    signal = lax.fori_loop(0, event_count, add_event, jnp.zeros((PATCH_X, PATCH_Y, SAMPLES), jnp.float32))
    noise_part = jax.random.truncated_normal(subkeys[5], -4.0, 4.0, (PATCH_X, PATCH_Y, SAMPLES), jnp.float32)
    return (signal + noise_part).astype(jnp.bfloat16)


def noise(key, extent, deviation, bound, kind=jnp.bfloat16):
    drawn = jax.random.normal(key, extent, jnp.float32) * deviation
    return jnp.minimum(jnp.maximum(drawn, -bound), bound).astype(kind)


def setup_inputs(seed: int = 0) -> dict:
    key_list = jax.random.split(jax.random.key(seed), 3)
    traces = draw_traces(jax.random.fold_in(key_list[2], 71), 0)
    omega = noise(key_list[1], (2, LAG_X, LAG_Y, RANK), (LAG_X * LAG_Y) ** -0.5, 0.125, jnp.float32)
    return dict(traces=traces, omega=omega)


highest = lax.Precision.HIGHEST

def fourier_tables(samples, freq_total):
    moments = jnp.arange(samples, dtype=jnp.int32)
    bins = jnp.arange(freq_total, dtype=jnp.int32) + 1
    phases = bins[:, None] * moments[None, :] % samples
    angles = phases.astype(jnp.float32) * (2.0 * math.pi / samples)
    return (jnp.cos(angles), jnp.sin(angles))

def anti_counts(spots, length, window, lags):
    counted = jnp.minimum(jnp.minimum(spots + 1, length - spots), min(window, lags))
    return counted.astype(jnp.float32)

def hankel_lags(source, window, lags):
    return jnp.stack([source[..., anchor:anchor + lags] for anchor in range(window)], axis=-2)

def denoise_slice(spec_pair, omega_one, omega_two, counts):
    spec_re, spec_im = spec_pair
    lagged_re = hankel_lags(spec_re, WIN_Y, LAG_Y)
    lagged_im = hankel_lags(spec_im, WIN_Y, LAG_Y)
    block_re = jnp.stack([lagged_re[anchor:anchor + WIN_X] for anchor in range(LAG_X)], axis=0)
    block_im = jnp.stack([lagged_im[anchor:anchor + WIN_X] for anchor in range(LAG_X)], axis=0)
    sketch = jnp.einsum('cabd,cdq->abq', block_re, omega_one, precision=highest) + jnp.einsum('cabd,cdq->abq', block_im, omega_two, precision=highest)
    inner = jnp.einsum('abp,abq->pq', sketch, sketch, precision=highest)
    gram_re = inner[:RANK, :RANK] + inner[RANK:, RANK:]
    gram_im = inner[:RANK, RANK:] - inner[RANK:, :RANK]
    real_gram = jnp.concatenate([jnp.concatenate([gram_re, -gram_im], 1), jnp.concatenate([gram_im, gram_re], 1)], 0)
    with_re = jnp.einsum('abq,cabd->qcd', sketch, block_re, precision=highest)
    with_im = jnp.einsum('abq,cabd->qcd', sketch, block_im, precision=highest)
    project_re = with_re[:RANK] + with_im[RANK:]
    project_im = with_im[:RANK] - with_re[RANK:]
    right_side = jnp.concatenate([project_re, project_im], 0).reshape(2 * RANK, LAG_X * LAG_Y)
    factor = jnp.linalg.cholesky(real_gram)
    solved = jax.scipy.linalg.cho_solve((factor, True), right_side)
    mix_re = solved[:RANK]
    mix_im = solved[RANK:]
    mixing = jnp.stack([jnp.concatenate([mix_re, -mix_im], 0), jnp.concatenate([mix_im, mix_re], 0)], -1).reshape(2 * RANK, LAG_X, LAG_Y, 2)
    zero_index = jnp.zeros((), jnp.int32)

    def add_lag(running, lag_index):
        column = lax.dynamic_index_in_dim(mixing, lag_index, 1, keepdims=False)
        lowrank = jnp.einsum('abq,qdz->abdz', sketch, column, precision=highest)
        spread = jnp.zeros((WIN_X, PATCH_Y, 2), jnp.float32)
        for shift_y in range(LAG_Y):
            spread = spread + jnp.pad(lowrank[:, :, shift_y], ((0, 0), (shift_y, LAG_Y - 1 - shift_y), (0, 0)))
        placed = lax.dynamic_update_slice(jnp.zeros((PATCH_X, PATCH_Y, 2), jnp.float32), spread, (lag_index, zero_index, zero_index))
        return (running + placed, None)
    running, unused = lax.scan(add_lag, jnp.zeros((PATCH_X, PATCH_Y, 2), jnp.float32), jnp.arange(LAG_X, dtype=jnp.int32))
    averaged = running / counts[:, :, None]
    return (averaged[:, :, 0], averaged[:, :, 1])

def reference(traces, omega):
    cosine_table, sine_table = fourier_tables(SAMPLES, FREQS)
    norm_scale = 1.0 / math.sqrt(SAMPLES)
    data = traces.astype(jnp.float32)
    spec_re = jnp.einsum('xyt,kt->kxy', data, cosine_table, precision=highest) * norm_scale
    spec_im = jnp.einsum('xyt,kt->kxy', data, sine_table, precision=highest) * -norm_scale
    omega_one = jnp.concatenate([omega[0], omega[1]], axis=-1)
    omega_two = jnp.concatenate([-omega[1], omega[0]], axis=-1)
    counts = anti_counts(jnp.arange(PATCH_X, dtype=jnp.int32), PATCH_X, WIN_X, LAG_X)[:, None] * anti_counts(jnp.arange(PATCH_Y, dtype=jnp.int32), PATCH_Y, WIN_Y, LAG_Y)[None, :]

    def per_bin(spec_pair):
        return denoise_slice(spec_pair, omega_one, omega_two, counts)
    avg_re, avg_im = lax.map(per_bin, (spec_re, spec_im))
    denoised = (jnp.einsum('kxy,kt->xyt', avg_re, cosine_table, precision=highest) - jnp.einsum('kxy,kt->xyt', avg_im, sine_table, precision=highest)) * (2.0 * norm_scale)
    return denoised
```

```python
import math

import jax
import jax.numpy as jnp
from jax import lax
from jax.sharding import PartitionSpec as P


highest = lax.Precision.HIGHEST


def fourier_tables(samples, freq_total):
    moments = jnp.arange(samples, dtype=jnp.int32)
    bins = jnp.arange(freq_total, dtype=jnp.int32) + 1
    phases = bins[:, None] * moments[None, :] % samples
    angles = phases.astype(jnp.float32) * (2.0 * math.pi / samples)
    return (jnp.cos(angles), jnp.sin(angles))


def anti_counts(spots, length, window, lags):
    counted = jnp.minimum(jnp.minimum(spots + 1, length - spots), min(window, lags))
    return counted.astype(jnp.float32)


def conv1d(lhs, rhs):
    return lax.conv_general_dilated(
        lhs, rhs, (1,), "VALID", dimension_numbers=("NWC", "WIO", "NWC"), precision=highest
    )


def body(traces, omega):
    rows_dev, cols_dev, samples = traces.shape
    lag_x, lag_y, rank_size = (omega.shape[1], omega.shape[2], omega.shape[3])
    trace_count = lax.axis_size("trace")
    freq_count = lax.axis_size("freq")
    patch_x = rows_dev * trace_count
    patch_y = cols_dev * freq_count
    win_x = patch_x - lag_x + 1
    win_y = patch_y - lag_y + 1
    freq_total = freq_count
    position = lax.axis_index("trace")
    cosine_table, sine_table = fourier_tables(samples, freq_total)
    norm_scale = 1.0 / math.sqrt(samples)

    forward = jnp.stack([cosine_table.T, -sine_table.T], axis=1) * norm_scale
    spectrum = jnp.einsum("xyt,tpk->xypk", traces.astype(jnp.float32), forward, precision=highest)
    spectrum = lax.all_to_all(spectrum, "freq", split_axis=3, concat_axis=1, tiled=True)
    whole = lax.all_gather(spectrum[..., 0], "trace", axis=0, tiled=True)

    spots = jnp.arange(win_y, dtype=jnp.int32)[:, None] + jnp.arange(lag_y, dtype=jnp.int32)[None, :]
    lagged = jnp.take(jnp.transpose(whole, (0, 2, 1)), spots, axis=2)
    sketch_in = jnp.transpose(lagged, (2, 0, 1, 3)).reshape(win_y, patch_x, 2 * lag_y)
    project_in = jnp.transpose(lagged, (1, 3, 0, 2)).reshape(2 * lag_y, patch_x, win_y)

    omega_one = jnp.concatenate([omega[0], omega[1]], axis=-1)
    omega_two = jnp.concatenate([-omega[1], omega[0]], axis=-1)
    kernel = jnp.stack([omega_one, omega_two], axis=1).reshape(lag_x, 2 * lag_y, 2 * rank_size)
    sketch = conv1d(sketch_in, kernel)

    inner = jnp.einsum("bap,baq->pq", sketch, sketch, precision=highest)
    gram_re = inner[:rank_size, :rank_size] + inner[rank_size:, rank_size:]
    gram_im = inner[:rank_size, rank_size:] - inner[rank_size:, :rank_size]
    real_gram = jnp.concatenate(
        [jnp.concatenate([gram_re, -gram_im], 1), jnp.concatenate([gram_im, gram_re], 1)], 0
    )

    with_all = conv1d(project_in, jnp.transpose(sketch, (1, 0, 2)))
    with_all = with_all.reshape(2, lag_y, lag_x, 2 * rank_size)
    with_re = jnp.transpose(with_all[0], (2, 1, 0))
    with_im = jnp.transpose(with_all[1], (2, 1, 0))
    project_re = with_re[:rank_size] + with_im[rank_size:]
    project_im = with_im[:rank_size] - with_re[rank_size:]
    right_side = jnp.concatenate([project_re, project_im], 0).reshape(2 * rank_size, lag_x * lag_y)

    factor = jnp.linalg.cholesky(real_gram)
    inverse_gram = jax.scipy.linalg.cho_solve((factor, True), jnp.eye(2 * rank_size, dtype=jnp.float32))
    solved = jnp.dot(inverse_gram, right_side, precision=highest)
    mix_re = solved[:rank_size]
    mix_im = solved[rank_size:]
    mixing = jnp.stack(
        [jnp.concatenate([mix_re, -mix_im], 0), jnp.concatenate([mix_im, mix_re], 0)], -1
    ).reshape(2 * rank_size, lag_x, lag_y, 2)

    first_row = position * rows_dev
    reach = win_x - 1
    padded = jnp.pad(mixing, ((0, 0), (reach, patch_x - lag_x), (0, 0), (0, 0)))
    window = lax.dynamic_slice_in_dim(padded, first_row, reach + rows_dev, 1)
    diag = (
        spots[:, :, None] == jnp.arange(patch_y, dtype=jnp.int32)[None, None, :]
    ).astype(jnp.float32)
    rows = []
    for r in range(rows_dev):
        picked = window[:, r : r + win_x][:, ::-1]
        spread = jnp.einsum("baq,qadz->bdz", sketch, picked, precision=highest)
        rows.append(jnp.einsum("bdz,bdy->zy", spread, diag, precision=highest))
    partial_value = jnp.stack(rows, 0)

    spots_x = first_row + jnp.arange(rows_dev, dtype=jnp.int32)
    spots_y = jnp.arange(patch_y, dtype=jnp.int32)
    counts = (
        anti_counts(spots_x, patch_x, win_x, lag_x)[:, None, None]
        * anti_counts(spots_y, patch_y, win_y, lag_y)[None, None, :]
    )
    averaged = (partial_value / counts)[:, None]
    returned = lax.all_to_all(averaged, "freq", split_axis=3, concat_axis=1, tiled=True)
    inverse = jnp.stack([cosine_table, -sine_table], axis=1) * (2.0 * norm_scale)
    return jnp.einsum("xkpy,kpt->xyt", returned, inverse, precision=highest)


def solution(mesh):
    return jax.shard_map(
        body,
        mesh=mesh,
        in_specs=(P("trace", "freq", None), P()),
        out_specs=P("trace", "freq", None),
        check_vma=False,
    )
```

```python
import math

import jax
import jax.numpy as jnp
from jax import lax
from jax.sharding import PartitionSpec as P


highest = lax.Precision.HIGHEST
fast = lax.Precision.HIGH


def fourier_tables(samples, freq_total):
    moments = jnp.arange(samples, dtype=jnp.int32)
    bins = jnp.arange(freq_total, dtype=jnp.int32) + 1
    phases = bins[:, None] * moments[None, :] % samples
    angles = phases.astype(jnp.float32) * (2.0 * math.pi / samples)
    return (jnp.cos(angles), jnp.sin(angles))


def anti_counts(spots, length, window, lags):
    counted = jnp.minimum(jnp.minimum(spots + 1, length - spots), min(window, lags))
    return counted.astype(jnp.float32)


def conv1d(lhs, rhs):
    return lax.conv_general_dilated(
        lhs, rhs, (1,), "VALID", dimension_numbers=("NWC", "WIO", "NWC"), precision=fast
    )


def body(traces, omega):
    rows_dev, cols_dev, samples = traces.shape
    lag_x, lag_y, rank_size = (omega.shape[1], omega.shape[2], omega.shape[3])
    trace_count = lax.axis_size("trace")
    freq_count = lax.axis_size("freq")
    patch_x = rows_dev * trace_count
    patch_y = cols_dev * freq_count
    win_x = patch_x - lag_x + 1
    win_y = patch_y - lag_y + 1
    freq_total = freq_count
    position = lax.axis_index("trace")
    cosine_table, sine_table = fourier_tables(samples, freq_total)
    norm_scale = 1.0 / math.sqrt(samples)

    forward = jnp.stack([cosine_table.T, -sine_table.T], axis=1) * norm_scale
    spectrum = jnp.einsum("xyt,tpk->xypk", traces.astype(jnp.float32), forward, precision=highest)
    spectrum = lax.all_to_all(spectrum, "freq", split_axis=3, concat_axis=1, tiled=True)
    own = spectrum[..., 0]
    copies = jnp.broadcast_to(own[None], (trace_count,) + own.shape)
    whole = lax.all_to_all(copies, "trace", split_axis=0, concat_axis=0, tiled=True)
    whole = whole.reshape(patch_x, patch_y, 2)

    spots = jnp.arange(win_y, dtype=jnp.int32)[:, None] + jnp.arange(lag_y, dtype=jnp.int32)[None, :]
    lagged = jnp.transpose(whole, (1, 0, 2))[spots]
    sketch_in = jnp.transpose(lagged, (0, 2, 3, 1)).reshape(win_y, patch_x, 2 * lag_y)
    project_in = jnp.transpose(lagged, (1, 2, 3, 0)).reshape(lag_y, patch_x, 2 * win_y)

    omega_one = jnp.concatenate([omega[0], omega[1]], axis=-1)
    omega_two = jnp.concatenate([-omega[1], omega[0]], axis=-1)
    kernel = jnp.stack([omega_one, omega_two], axis=1).reshape(lag_x, 2 * lag_y, 2 * rank_size)
    sketch = conv1d(sketch_in, kernel)

    inner = jnp.einsum("bap,baq->pq", sketch, sketch, precision=fast)
    gram_re = inner[:rank_size, :rank_size] + inner[rank_size:, rank_size:]
    gram_im = inner[:rank_size, rank_size:] - inner[rank_size:, :rank_size]
    real_gram = jnp.concatenate(
        [jnp.concatenate([gram_re, -gram_im], 1), jnp.concatenate([gram_im, gram_re], 1)], 0
    )

    sketch_re = sketch[..., :rank_size]
    sketch_im = sketch[..., rank_size:]
    taps = jnp.stack(
        [
            jnp.concatenate([sketch_re, -sketch_im], -1),
            jnp.concatenate([sketch_im, sketch_re], -1),
        ],
        0,
    )
    taps = jnp.transpose(taps, (2, 0, 1, 3)).reshape(win_x, 2 * win_y, 2 * rank_size)
    projected = conv1d(project_in, taps)
    right_side = jnp.transpose(projected, (2, 1, 0)).reshape(2 * rank_size, lag_x * lag_y)

    factor = jnp.linalg.cholesky(real_gram)
    inverse_gram = jax.scipy.linalg.cho_solve((factor, True), jnp.eye(2 * rank_size, dtype=jnp.float32))
    solved = jnp.dot(inverse_gram, right_side, precision=fast)
    mix_re = solved[:rank_size]
    mix_im = solved[rank_size:]
    mixing = jnp.stack(
        [jnp.concatenate([mix_re, -mix_im], 0), jnp.concatenate([mix_im, mix_re], 0)], -1
    ).reshape(2 * rank_size, lag_x, lag_y, 2)

    first_row = position * rows_dev
    reach = win_x - 1
    padded = jnp.pad(mixing, ((0, 0), (reach, patch_x - lag_x), (0, 0), (0, 0)))
    window = lax.dynamic_slice_in_dim(padded, first_row, reach + rows_dev, 1)
    diag = (
        spots[:, :, None] == jnp.arange(patch_y, dtype=jnp.int32)[None, None, :]
    ).astype(jnp.float32)
    rows = []
    for r in range(rows_dev):
        picked = window[:, r : r + win_x][:, ::-1]
        spread = jnp.einsum("baq,qadz->bdz", sketch, picked, precision=fast)
        rows.append(jnp.einsum("bdz,bdy->zy", spread, diag, precision=fast))
    partial_value = jnp.stack(rows, 0)

    spots_x = first_row + jnp.arange(rows_dev, dtype=jnp.int32)
    spots_y = jnp.arange(patch_y, dtype=jnp.int32)
    counts = (
        anti_counts(spots_x, patch_x, win_x, lag_x)[:, None, None]
        * anti_counts(spots_y, patch_y, win_y, lag_y)[None, None, :]
    )
    averaged = (partial_value / counts)[:, None]
    returned = lax.all_to_all(averaged, "freq", split_axis=3, concat_axis=1, tiled=True)
    inverse = jnp.stack([cosine_table, -sine_table], axis=1) * (2.0 * norm_scale)
    return jnp.einsum("xkpy,kpt->xyt", returned, inverse, precision=highest)


def solution(mesh):
    return jax.shard_map(
        body,
        mesh=mesh,
        in_specs=(P("trace", "freq", None), P()),
        out_specs=P("trace", "freq", None),
        check_vma=False,
    )
```

```python
import math

import jax
import jax.numpy as jnp
from jax import lax
from jax.sharding import PartitionSpec as P


highest = lax.Precision.HIGHEST
fast = lax.Precision.HIGH


def fourier_tables(samples, freq_total):
    moments = jnp.arange(samples, dtype=jnp.int32)
    bins = jnp.arange(freq_total, dtype=jnp.int32) + 1
    phases = bins[:, None] * moments[None, :] % samples
    angles = phases.astype(jnp.float32) * (2.0 * math.pi / samples)
    return (jnp.cos(angles), jnp.sin(angles))


def anti_counts(spots, length, window, lags):
    counted = jnp.minimum(jnp.minimum(spots + 1, length - spots), min(window, lags))
    return counted.astype(jnp.float32)


def conv1d(lhs, rhs):
    return lax.conv_general_dilated(
        lhs, rhs, (1,), "VALID", dimension_numbers=("NWC", "WIO", "NWC"), precision=highest
    )


def body(traces, omega):
    rows_dev, cols_dev, samples = traces.shape
    lag_x, lag_y, rank_size = (omega.shape[1], omega.shape[2], omega.shape[3])
    trace_count = lax.axis_size("trace")
    freq_count = lax.axis_size("freq")
    patch_x = rows_dev * trace_count
    patch_y = cols_dev * freq_count
    win_x = patch_x - lag_x + 1
    win_y = patch_y - lag_y + 1
    freq_total = freq_count
    position = lax.axis_index("trace")
    cosine_table, sine_table = fourier_tables(samples, freq_total)
    norm_scale = 1.0 / math.sqrt(samples)

    forward = jnp.stack([cosine_table.T, -sine_table.T], axis=1) * norm_scale
    spectrum = jnp.einsum("xyt,tpk->xypk", traces.astype(jnp.float32), forward, precision=highest)
    spectrum = lax.all_to_all(spectrum, "freq", split_axis=3, concat_axis=1, tiled=True)
    own = spectrum[..., 0]
    copies = jnp.broadcast_to(own[None], (trace_count,) + own.shape)
    whole = lax.all_to_all(copies, "trace", split_axis=0, concat_axis=0, tiled=True)
    whole = whole.reshape(patch_x, patch_y, 2)

    spots = jnp.arange(win_y, dtype=jnp.int32)[:, None] + jnp.arange(lag_y, dtype=jnp.int32)[None, :]
    lagged = jnp.transpose(whole, (1, 0, 2))[spots]
    sketch_in = jnp.transpose(lagged, (0, 2, 3, 1)).reshape(win_y, patch_x, 2 * lag_y)
    project_in = jnp.transpose(lagged, (1, 2, 3, 0)).reshape(lag_y, patch_x, 2 * win_y)

    omega_one = jnp.concatenate([omega[0], omega[1]], axis=-1)
    omega_two = jnp.concatenate([-omega[1], omega[0]], axis=-1)
    kernel = jnp.stack([omega_one, omega_two], axis=1).reshape(lag_x, 2 * lag_y, 2 * rank_size)
    sketch = conv1d(sketch_in, kernel)

    inner = jnp.einsum("bap,baq->pq", sketch, sketch, precision=fast)
    gram_re = inner[:rank_size, :rank_size] + inner[rank_size:, rank_size:]
    gram_im = inner[:rank_size, rank_size:] - inner[rank_size:, :rank_size]
    real_gram = jnp.concatenate(
        [jnp.concatenate([gram_re, -gram_im], 1), jnp.concatenate([gram_im, gram_re], 1)], 0
    )

    sketch_re = sketch[..., :rank_size]
    sketch_im = sketch[..., rank_size:]
    taps = jnp.stack(
        [
            jnp.concatenate([sketch_re, -sketch_im], -1),
            jnp.concatenate([sketch_im, sketch_re], -1),
        ],
        0,
    )
    taps = jnp.transpose(taps, (2, 0, 1, 3)).reshape(win_x, 2 * win_y, 2 * rank_size)
    projected = conv1d(project_in, taps)
    right_side = jnp.transpose(projected, (2, 1, 0)).reshape(2 * rank_size, lag_x * lag_y)

    factor = jnp.linalg.cholesky(real_gram)
    inverse_gram = jax.scipy.linalg.cho_solve((factor, True), jnp.eye(2 * rank_size, dtype=jnp.float32))
    solved = jnp.dot(inverse_gram, right_side, precision=fast)
    mix_re = solved[:rank_size]
    mix_im = solved[rank_size:]
    mixing = jnp.stack(
        [jnp.concatenate([mix_re, -mix_im], 0), jnp.concatenate([mix_im, mix_re], 0)], -1
    ).reshape(2 * rank_size, lag_x, lag_y, 2)

    first_row = position * rows_dev
    reach = win_x - 1
    padded = jnp.pad(mixing, ((0, 0), (reach, patch_x - lag_x), (0, 0), (0, 0)))
    window = lax.dynamic_slice_in_dim(padded, first_row, reach + rows_dev, 1)
    diag = (
        spots[:, :, None] == jnp.arange(patch_y, dtype=jnp.int32)[None, None, :]
    ).astype(jnp.float32)
    rows = []
    for r in range(rows_dev):
        picked = window[:, r : r + win_x][:, ::-1]
        spread = jnp.einsum("baq,qadz->bdz", sketch, picked, precision=fast)
        rows.append(jnp.einsum("bdz,bdy->zy", spread, diag, precision=fast))
    partial_value = jnp.stack(rows, 0)

    spots_x = first_row + jnp.arange(rows_dev, dtype=jnp.int32)
    spots_y = jnp.arange(patch_y, dtype=jnp.int32)
    counts = (
        anti_counts(spots_x, patch_x, win_x, lag_x)[:, None, None]
        * anti_counts(spots_y, patch_y, win_y, lag_y)[None, None, :]
    )
    averaged = (partial_value / counts)[:, None]
    returned = lax.all_to_all(averaged, "freq", split_axis=3, concat_axis=1, tiled=True)
    inverse = jnp.stack([cosine_table, -sine_table], axis=1) * (2.0 * norm_scale)
    return jnp.einsum("xkpy,kpt->xyt", returned, inverse, precision=highest)


def solution(mesh):
    return jax.shard_map(
        body,
        mesh=mesh,
        in_specs=(P("trace", "freq", None), P()),
        out_specs=P("trace", "freq", None),
        check_vma=False,
    )
```

```python
import math

import jax
import jax.numpy as jnp
from jax import lax
from jax.sharding import PartitionSpec as P


highest = lax.Precision.HIGHEST


def fourier_tables(samples, freq_total):
    moments = jnp.arange(samples, dtype=jnp.int32)
    bins = jnp.arange(freq_total, dtype=jnp.int32) + 1
    phases = bins[:, None] * moments[None, :] % samples
    angles = phases.astype(jnp.float32) * (2.0 * math.pi / samples)
    return (jnp.cos(angles), jnp.sin(angles))


def anti_counts(spots, length, window, lags):
    counted = jnp.minimum(jnp.minimum(spots + 1, length - spots), min(window, lags))
    return counted.astype(jnp.float32)


def conv1d(lhs, rhs):
    return lax.conv_general_dilated(
        lhs, rhs, (1,), "VALID", dimension_numbers=("NWC", "WIO", "NWC"), precision=highest
    )


def body(traces, omega):
    rows_dev, cols_dev, samples = traces.shape
    lag_x, lag_y, rank_size = (omega.shape[1], omega.shape[2], omega.shape[3])
    trace_count = lax.axis_size("trace")
    freq_count = lax.axis_size("freq")
    patch_x = rows_dev * trace_count
    patch_y = cols_dev * freq_count
    win_x = patch_x - lag_x + 1
    win_y = patch_y - lag_y + 1
    freq_total = freq_count
    position = lax.axis_index("trace")
    cosine_table, sine_table = fourier_tables(samples, freq_total)
    norm_scale = 1.0 / math.sqrt(samples)

    forward = jnp.stack([cosine_table.T, -sine_table.T], axis=1) * norm_scale
    spectrum = jnp.einsum("xyt,tpk->xypk", traces.astype(jnp.float32), forward, precision=highest)
    spectrum = lax.all_to_all(spectrum, "freq", split_axis=3, concat_axis=1, tiled=True)
    own = spectrum[..., 0]
    copies = jnp.broadcast_to(own[None], (trace_count,) + own.shape)
    whole = lax.all_to_all(copies, "trace", split_axis=0, concat_axis=0, tiled=True)
    whole = whole.reshape(patch_x, patch_y, 2)

    spots = jnp.arange(win_y, dtype=jnp.int32)[:, None] + jnp.arange(lag_y, dtype=jnp.int32)[None, :]
    lagged = jnp.transpose(whole, (1, 0, 2))[spots]
    sketch_in = jnp.transpose(lagged, (0, 2, 3, 1)).reshape(win_y, patch_x, 2 * lag_y)
    project_in = jnp.transpose(lagged, (1, 2, 3, 0)).reshape(lag_y, patch_x, 2 * win_y)

    omega_one = jnp.concatenate([omega[0], omega[1]], axis=-1)
    omega_two = jnp.concatenate([-omega[1], omega[0]], axis=-1)
    kernel = jnp.stack([omega_one, omega_two], axis=1).reshape(lag_x, 2 * lag_y, 2 * rank_size)
    sketch = conv1d(sketch_in, kernel)

    inner = jnp.einsum("bap,baq->pq", sketch, sketch, precision=highest)
    gram_re = inner[:rank_size, :rank_size] + inner[rank_size:, rank_size:]
    gram_im = inner[:rank_size, rank_size:] - inner[rank_size:, :rank_size]
    real_gram = jnp.concatenate(
        [jnp.concatenate([gram_re, -gram_im], 1), jnp.concatenate([gram_im, gram_re], 1)], 0
    )

    sketch_re = sketch[..., :rank_size]
    sketch_im = sketch[..., rank_size:]
    taps = jnp.stack(
        [
            jnp.concatenate([sketch_re, -sketch_im], -1),
            jnp.concatenate([sketch_im, sketch_re], -1),
        ],
        0,
    )
    taps = jnp.transpose(taps, (2, 0, 1, 3)).reshape(win_x, 2 * win_y, 2 * rank_size)
    projected = conv1d(project_in, taps)
    right_side = jnp.transpose(projected, (2, 1, 0)).reshape(2 * rank_size, lag_x * lag_y)

    factor = jnp.linalg.cholesky(real_gram)
    inverse_gram = jax.scipy.linalg.cho_solve((factor, True), jnp.eye(2 * rank_size, dtype=jnp.float32))
    solved = jnp.dot(inverse_gram, right_side, precision=highest)
    mix_re = solved[:rank_size]
    mix_im = solved[rank_size:]
    mixing = jnp.stack(
        [jnp.concatenate([mix_re, -mix_im], 0), jnp.concatenate([mix_im, mix_re], 0)], -1
    ).reshape(2 * rank_size, lag_x, lag_y, 2)

    first_row = position * rows_dev
    reach = win_x - 1
    padded = jnp.pad(mixing, ((0, 0), (reach, patch_x - lag_x), (0, 0), (0, 0)))
    window = lax.dynamic_slice_in_dim(padded, first_row, reach + rows_dev, 1)
    diag = (
        spots[:, :, None] == jnp.arange(patch_y, dtype=jnp.int32)[None, None, :]
    ).astype(jnp.float32)
    rows = []
    for r in range(rows_dev):
        picked = window[:, r : r + win_x][:, ::-1]
        spread = jnp.einsum("baq,qadz->bdz", sketch, picked, precision=highest)
        rows.append(jnp.einsum("bdz,bdy->zy", spread, diag, precision=highest))
    partial_value = jnp.stack(rows, 0)

    spots_x = first_row + jnp.arange(rows_dev, dtype=jnp.int32)
    spots_y = jnp.arange(patch_y, dtype=jnp.int32)
    counts = (
        anti_counts(spots_x, patch_x, win_x, lag_x)[:, None, None]
        * anti_counts(spots_y, patch_y, win_y, lag_y)[None, None, :]
    )
    averaged = (partial_value / counts)[:, None]
    returned = lax.all_to_all(averaged, "freq", split_axis=3, concat_axis=1, tiled=True)
    inverse = jnp.stack([cosine_table, -sine_table], axis=1) * (2.0 * norm_scale)
    return jnp.einsum("xkpy,kpt->xyt", returned, inverse, precision=highest)


def solution(mesh):
    return jax.shard_map(
        body,
        mesh=mesh,
        in_specs=(P("trace", "freq", None), P()),
        out_specs=P("trace", "freq", None),
        check_vma=False,
    )
```

```python
import math

import jax
import jax.numpy as jnp
from jax import lax
from jax.sharding import PartitionSpec as P


highest = lax.Precision.HIGHEST


def fourier_tables(samples, freq_total):
    moments = jnp.arange(samples, dtype=jnp.int32)
    bins = jnp.arange(freq_total, dtype=jnp.int32) + 1
    phases = bins[:, None] * moments[None, :] % samples
    angles = phases.astype(jnp.float32) * (2.0 * math.pi / samples)
    return (jnp.cos(angles), jnp.sin(angles))


def anti_counts(spots, length, window, lags):
    counted = jnp.minimum(jnp.minimum(spots + 1, length - spots), min(window, lags))
    return counted.astype(jnp.float32)


def conv1d(lhs, rhs, lhs_spec):
    return lax.conv_general_dilated(
        lhs, rhs, (1,), "VALID", dimension_numbers=(lhs_spec, "WIO", "NWC"), precision=highest
    )


def body(traces, omega):
    rows_dev, cols_dev, samples = traces.shape
    lag_x, lag_y, rank_size = (omega.shape[1], omega.shape[2], omega.shape[3])
    trace_count = lax.axis_size("trace")
    freq_count = lax.axis_size("freq")
    patch_x = rows_dev * trace_count
    patch_y = cols_dev * freq_count
    win_x = patch_x - lag_x + 1
    win_y = patch_y - lag_y + 1
    freq_total = freq_count
    position = lax.axis_index("trace")
    cosine_table, sine_table = fourier_tables(samples, freq_total)
    norm_scale = 1.0 / math.sqrt(samples)

    forward = jnp.stack([cosine_table.T, -sine_table.T], axis=1) * norm_scale
    spectrum = jnp.einsum("xyt,tpk->xypk", traces.astype(jnp.float32), forward, precision=highest)
    spectrum = lax.all_to_all(spectrum, "freq", split_axis=3, concat_axis=1, tiled=True)
    own = spectrum[..., 0]
    copies = jnp.broadcast_to(own[None], (trace_count,) + own.shape)
    whole = lax.all_to_all(copies, "trace", split_axis=0, concat_axis=0, tiled=True)
    whole = whole.reshape(patch_x, patch_y, 2)

    spots = jnp.arange(win_y, dtype=jnp.int32)[:, None] + jnp.arange(lag_y, dtype=jnp.int32)[None, :]
    lagged_re = jnp.transpose(whole[:, :, 0])[spots]
    lagged_im = jnp.transpose(whole[:, :, 1])[spots]
    sketch_in = jnp.concatenate([lagged_re, lagged_im], axis=1)
    project_in = jnp.concatenate([lagged_re, lagged_im], axis=0)

    omega_one = jnp.concatenate([omega[0], omega[1]], axis=-1)
    omega_two = jnp.concatenate([-omega[1], omega[0]], axis=-1)
    kernel = jnp.stack([omega_one, omega_two], axis=1).reshape(lag_x, 2 * lag_y, 2 * rank_size)
    sketch = conv1d(sketch_in, kernel, "NCW")

    inner = jnp.einsum("bap,baq->pq", sketch, sketch, precision=highest)
    gram_re = inner[:rank_size, :rank_size] + inner[rank_size:, rank_size:]
    gram_im = inner[:rank_size, rank_size:] - inner[rank_size:, :rank_size]
    real_gram = jnp.concatenate(
        [jnp.concatenate([gram_re, -gram_im], 1), jnp.concatenate([gram_im, gram_re], 1)], 0
    )

    sketch_re = sketch[..., :rank_size]
    sketch_im = sketch[..., rank_size:]
    taps = jnp.stack(
        [
            jnp.concatenate([sketch_re, -sketch_im], -1),
            jnp.concatenate([sketch_im, sketch_re], -1),
        ],
        0,
    )
    taps = jnp.transpose(taps, (2, 0, 1, 3)).reshape(win_x, 2 * win_y, 2 * rank_size)
    projected = conv1d(project_in, taps, "CNW")
    right_side = jnp.transpose(projected, (2, 1, 0)).reshape(2 * rank_size, lag_x * lag_y)

    factor = jnp.linalg.cholesky(real_gram)
    inverse_gram = jax.scipy.linalg.cho_solve((factor, True), jnp.eye(2 * rank_size, dtype=jnp.float32))
    solved = jnp.dot(inverse_gram, right_side, precision=highest)
    mix_re = solved[:rank_size]
    mix_im = solved[rank_size:]
    mixing = jnp.stack(
        [jnp.concatenate([mix_re, -mix_im], 0), jnp.concatenate([mix_im, mix_re], 0)], -1
    ).reshape(2 * rank_size, lag_x, lag_y, 2)

    first_row = position * rows_dev
    reach = win_x - 1
    padded = jnp.pad(mixing, ((0, 0), (reach, patch_x - lag_x), (0, 0), (0, 0)))
    window = lax.dynamic_slice_in_dim(padded, first_row, reach + rows_dev, 1)
    diag = (
        spots[:, :, None] == jnp.arange(patch_y, dtype=jnp.int32)[None, None, :]
    ).astype(jnp.float32)
    rows = []
    for r in range(rows_dev):
        picked = window[:, r : r + win_x][:, ::-1]
        spread = jnp.einsum("baq,qadz->bdz", sketch, picked, precision=highest)
        rows.append(jnp.einsum("bdz,bdy->zy", spread, diag, precision=highest))
    partial_value = jnp.stack(rows, 0)

    spots_x = first_row + jnp.arange(rows_dev, dtype=jnp.int32)
    spots_y = jnp.arange(patch_y, dtype=jnp.int32)
    counts = (
        anti_counts(spots_x, patch_x, win_x, lag_x)[:, None, None]
        * anti_counts(spots_y, patch_y, win_y, lag_y)[None, None, :]
    )
    averaged = (partial_value / counts)[:, None]
    returned = lax.all_to_all(averaged, "freq", split_axis=3, concat_axis=1, tiled=True)
    inverse = jnp.stack([cosine_table, -sine_table], axis=1) * (2.0 * norm_scale)
    return jnp.einsum("xkpy,kpt->xyt", returned, inverse, precision=highest)


def solution(mesh):
    return jax.shard_map(
        body,
        mesh=mesh,
        in_specs=(P("trace", "freq", None), P()),
        out_specs=P("trace", "freq", None),
        check_vma=False,
    )
```
